128 devices in a mesh: blk: 2 (over core), span: 4 (over x), inst: 16 (over z, y).
Axes of the slice: x: 4, y: 4, z: 4, core: 2. Of those that a mesh axis runs over, the one named last changes fastest.
Arguments:
- source: bfloat16 [16, 16, 81920], P('inst', None, ('blk', 'span')), may hold values from -6 to 6
- jac_interior: bfloat16 [128, 10, 320, 320], P(('blk', 'span', 'inst')), may hold values from -0.25 to 0.25
- interior_rows: int32 [128, 10], P(('blk', 'span', 'inst')), may hold values from 0 to 31
- interior_cols: int32 [128, 10], P(('blk', 'span', 'inst')), may hold values from 0 to 31
- jac_face: bfloat16 [128, 8, 320, 320], P(('blk', 'span', 'inst')), may hold values from -0.25 to 0.25
- face_rows: int32 [128, 8], P(('blk', 'span', 'inst')), may hold values from 0 to 31
- face_cols: int32 [128, 8], P(('blk', 'span', 'inst')), may hold values from 0 to 7, each once within a row
- face_map: int32 [4], replicated, may hold values from 0 to 3, each once
- frequency: float32 [1], replicated, may hold values from 0.04 to 0.1
- surf_mode: int32 [32768, 1], P(('blk', 'span', 'inst')), may hold values from 0 to 1; in each aligned block of 256 rows (0 to 255, 256 to 511, ...) at most 256 rows name the same one
- surf_row: int32 [128, 256], P(('blk', 'span', 'inst')), may hold values from 0 to 10239
- surf_node: int32 [128, 256], P(('blk', 'span', 'inst')), may hold values from 0 to 32767
- mode_shape: float32 [2, 32768], P('blk'), may hold values from -0.4375 to 0.4375
Outputs:
- adjoint: bfloat16 [16, 16, 81920], P('inst', None, ('blk', 'span'))
- modal_grad: float32 [16, 2, 16], P('inst', 'blk')
The draws below stay inside these ranges and needn't reach their ends.
Inputs may be any that keep to these rules, and one draw needn't show every extreme that they name: `surf_mode`: within the 256 entries of one device no mode is named by more than 256 entries, a bound that some block reaches. `face_cols`: each row names every number below 8 once. `face_map`: each number below 4 once.
All inputs are finite; a program needn't handle non-finite values.
Results may differ from the reference program's by a relative error of at most 0.0051.
Values may be sent and summed in bfloat16 or wider, within the bound.
No kernel may reach another device: no remote copies, remote signals or barrier semaphores. Data moves between devices by JAX's collectives and lax.ppermute only.
A program may use at most 64 MiB of HBM per device.

```python
import math
import jax
import jax.numpy as jnp
import numpy as np
from jax import lax

BS = 320
RHS = 16
MODES = 2
NB = 32
NI = 10
FB = 2
NF = 8
PF = 4
ITERS = 6
SURF = 256
CAP = 256
SURF_NODES = 32768
N_BLK = 2
N_SPAN = 4
N_INST = 16


def plant(result, stream_key, least, top_value):
    place = [jax.random.randint(jax.random.fold_in(stream_key, axis), (), 0, length) for axis, length in enumerate(result.shape)]
    widest = result.shape.index(max(result.shape))
    next_to = place[:widest] + [(place[widest] + 1) % result.shape[widest]] + place[widest + 1:]
    return result.at[tuple(place)].set(least).at[tuple(next_to)].set(top_value)


def block_levels(key, extent, cuts, low, high):
    def one(axis_at, shards_of):
        steps = jax.random.uniform(jax.random.fold_in(jax.random.fold_in(key, 6), axis_at), (shards_of,), jnp.float32, low / len(cuts), high / len(cuts))
        return jnp.repeat(jnp.exp(steps), extent[axis_at] // shards_of).reshape((-1,) + (1,) * (len(extent) - axis_at - 1))

    level = one(*cuts[0])
    for cut in cuts[1:]:
        level = level * one(*cut)
    return level


def shared_out(key, own, number, rows, count, top, bound, skew):
    order = jax.random.permutation(key, count)
    packed, usual = portions_of(count, rows * top, bound, skew, True), portions_of(count, rows * top, bound, skew, False)
    places = jnp.arange(count)

    def named(tallies, turn):
        used = int((tallies > 0).sum())
        fixed = max(1, used // 4)
        shifted = fixed + (places - fixed + turn * (used - fixed)) % max(1, count - fixed)
        return jnp.zeros((count,), jnp.int32).at[order[jnp.where(places < fixed, places, shifted)]].set(jnp.asarray(tallies, jnp.int32))

    tallies = jnp.where(number % 4 == 0, named(packed, number // 4), named(usual, number - number // 4 - 1))
    mixed = jax.random.permutation(jax.random.fold_in(own, 3), count)
    source_of, sink = mixed[0:count // 2 * 2:2], mixed[1:count // 2 * 2:2]
    margin = jnp.minimum(tallies[source_of] - 1, bound - tallies[sink]) // 2
    margin = jnp.where((source_of == order[0]) | (sink == order[0]) | (tallies[sink] == 0), 0, jnp.maximum(margin, 0))
    shifted = jax.random.randint(jax.random.fold_in(own, 4), (count // 2,), 0, 1 << 20) % (margin + 1)
    tallies = tallies.at[source_of].add(-shifted).at[sink].add(shifted)
    labels = jnp.searchsorted(jnp.cumsum(tallies), jnp.arange(rows * top), side="right").astype(jnp.int32)
    listing = labels.reshape(top, rows).T
    listing = listing[jax.random.permutation(jax.random.fold_in(own, 1), rows)]
    turn = jax.random.randint(jax.random.fold_in(own, 2), (rows, 1), 0, top)
    return jnp.take_along_axis(listing, (jnp.arange(top)[None, :] + turn) % top, axis=1)


def portions_of(amount, total, reach, slope, full):
    weights = [(1 << 20) // math.isqrt(standing ** slope) + 1 for standing in range(1, amount + 1)]
    largest = reach if full else min(reach, max(-(-total // amount), total * weights[0] // sum(weights)))
    least = 1 if total - largest >= amount - 1 else 0
    given, surplus = [largest] + [least] * (amount - 1), total - largest - least * (amount - 1)
    while surplus > 0:
        candidates = [i for i in range(1, amount) if given[i] < largest] or [i for i in range(1, amount) if given[i] < reach]
        whole, budget = sum([weights[i] for i in candidates]), surplus
        for i in candidates:
            more = min(reach - given[i], max(1, budget * weights[i] // whole), surplus)
            given[i] = given[i] + more
            surplus = surplus - more
    return np.array(given)


def bell_draw(stream_key, extent, deviation, limit, pieces=(), kind=jnp.bfloat16):
    entries = jax.random.normal(stream_key, extent, jnp.float32) * deviation
    if len(pieces) > 0:
        entries = block_levels(stream_key, extent, pieces, -0.22, 0.18) * entries
    return jnp.clip(entries, min=-limit, max=limit).astype(kind)


def setup_inputs(seed: int = 0) -> dict:
    splits = jax.random.split(jax.random.key(seed), 14)
    source = bell_draw(splits[0], (N_INST, RHS, N_BLK * N_SPAN * NB * BS), 1.0, 6.0, ((0, 16), (2, 8)))
    jac_interior = bell_draw(splits[1], (N_BLK * N_SPAN * N_INST, NI, BS, BS), (2 * BS) ** -0.5, 0.25, ((0, 128),))
    interior_rows = plant(jax.random.randint(splits[2], (N_BLK * N_SPAN * N_INST, NI), 0, NB), jax.random.fold_in(splits[2], 1), 0, NB - 1).astype(jnp.int32)
    interior_cols = plant(jax.random.randint(splits[3], (N_BLK * N_SPAN * N_INST, NI), 0, NB), jax.random.fold_in(splits[3], 1), 0, NB - 1).astype(jnp.int32)
    jac_face = bell_draw(splits[4], (N_BLK * N_SPAN * N_INST, NF, BS, BS), (2 * BS) ** -0.5, 0.25, ((0, 128),))
    face_rows = plant(jax.random.randint(splits[5], (N_BLK * N_SPAN * N_INST, NF), 0, NB), jax.random.fold_in(splits[5], 1), 0, NB - 1).astype(jnp.int32)
    face_cols = jax.vmap(lambda own: jax.random.permutation(own, NF))(jax.random.split(splits[6], (N_BLK * N_SPAN * N_INST))).reshape((N_BLK * N_SPAN * N_INST, NF)).astype(jnp.int32)
    face_map = jax.random.permutation(splits[7], PF).astype(jnp.int32)
    frequency = jnp.clip(jax.random.uniform(splits[8], (1,), jnp.float32, 0.04, 0.1), 0.04, 0.1)
    surf_mode_keys = jax.random.split(jax.random.fold_in(splits[9], 1), (N_BLK * N_SPAN * N_INST * SURF) // SURF)
    surf_mode_turns = jax.random.permutation(jax.random.fold_in(splits[9], 3), (N_BLK * N_SPAN * N_INST * SURF) // SURF)
    surf_mode = jax.vmap(lambda own, number: shared_out(jax.random.fold_in(splits[9], 2), own, number, SURF, MODES, 1, CAP, 2))(surf_mode_keys, surf_mode_turns).reshape((N_BLK * N_SPAN * N_INST * SURF, 1))
    surf_row = plant(jax.random.randint(splits[10], (N_BLK * N_SPAN * N_INST, SURF), 0, NB * BS), jax.random.fold_in(splits[10], 1), 0, (NB * BS) - 1).astype(jnp.int32)
    surf_node = plant(jax.random.randint(splits[11], (N_BLK * N_SPAN * N_INST, SURF), 0, SURF_NODES), jax.random.fold_in(splits[11], 1), 0, SURF_NODES - 1).astype(jnp.int32)
    mode_shape = bell_draw(splits[12], (MODES, SURF_NODES), 0.03, 0.4375, ((0, 2),), jnp.float32)
    return {"source": source, "jac_interior": jac_interior, "interior_rows": interior_rows, "interior_cols": interior_cols, "jac_face": jac_face, "face_rows": face_rows, "face_cols": face_cols, "face_map": face_map, "frequency": frequency, "surf_mode": surf_mode, "surf_row": surf_row, "surf_node": surf_node, "mode_shape": mode_shape}


def loop_weight(offset, inst_count):
    angle = math.pi * offset / inst_count
    parity = jnp.cos(math.pi * offset)
    sine_safe = jnp.where(offset == 0, 1.0, jnp.sin(angle))
    value = 0.5 * parity / sine_safe
    return jnp.where(offset == 0, 0.0, value)


def device_sweep(operands):
    own_blocks, face_sources, jac_in, rows_in, cols_in, jac_out, rows_out, cols_out = operands
    inner_prod = jnp.einsum('rnk,nkl->rnl', own_blocks[:, cols_in, :].astype(jnp.float32), jac_in.astype(jnp.float32), precision=lax.Precision.HIGHEST)
    outer_prod = jnp.einsum('rnk,nkl->rnl', face_sources[:, cols_out, :].astype(jnp.float32), jac_out.astype(jnp.float32), precision=lax.Precision.HIGHEST)
    summed = jnp.zeros(own_blocks.shape, jnp.float32).at[:, rows_in, :].add(inner_prod)
    return summed.at[:, rows_out, :].add(outer_prod)


def reference(source, jac_interior, interior_rows, interior_cols, jac_face, face_rows, face_cols, face_map, frequency, surf_mode, surf_row, surf_node, mode_shape):
    device_count = N_BLK * N_SPAN * N_INST
    shaped = (N_INST, RHS, N_BLK, N_SPAN, NB, BS)
    source_wide = source.astype(jnp.float32)
    offsets = jnp.arange(N_INST).astype(jnp.float32)
    loop_matrix = loop_weight(offsets[:, None] - offsets[None, :], N_INST)
    psi_now = source
    for sweep_step in range(ITERS):
        grid = psi_now.reshape(shaped)
        spectral = jnp.einsum('ji,jrc->irc', loop_matrix, psi_now.astype(jnp.float32), precision=lax.Precision.HIGHEST)
        prev_face = jnp.roll(grid[:, :, :, :, NB - FB:, :], 1, axis=2)
        next_face = jnp.roll(grid[:, :, :, :, :FB, :], -1, axis=2)
        passage = jnp.concatenate([prev_face, next_face], axis=4)[:, :, :, :, face_map, :]
        empty_slab = jnp.zeros_like(grid[:, :, :, :1, :FB, :])
        lower_rim = jnp.concatenate([empty_slab, grid[:, :, :, :-1, NB - FB:, :]], axis=3)
        upper_rim = jnp.concatenate([grid[:, :, :, 1:, :FB, :], empty_slab], axis=3)
        face_sources = jnp.concatenate([passage, lower_rim, upper_rim], axis=4)
        own_dev = grid.transpose(2, 3, 0, 1, 4, 5).reshape(device_count, RHS, NB, BS)
        face_dev = face_sources.transpose(2, 3, 0, 1, 4, 5).reshape(device_count, RHS, 4 * FB, BS)
        summed = lax.map(device_sweep, (own_dev, face_dev, jac_interior, interior_rows, interior_cols, jac_face, face_rows, face_cols))
        summed = summed.reshape(N_BLK, N_SPAN, N_INST, RHS, NB, BS).transpose(2, 3, 0, 1, 4, 5).reshape(source.shape)
        psi_now = (source_wide - summed - frequency[0] * spectral).astype(jnp.bfloat16)
    flat_dev = psi_now.reshape(N_INST, RHS, N_BLK, N_SPAN, NB * BS).transpose(2, 3, 0, 1, 4).reshape(device_count, RHS, NB * BS)
    loads = jnp.take_along_axis(flat_dev, surf_row[:, None, :], axis=2).astype(jnp.float32)
    modes_dev = surf_mode.reshape(device_count, SURF)
    picked = mode_shape[modes_dev, surf_node]
    terms = (loads * picked[:, None, :]).transpose(0, 2, 1)
    inst_of = jnp.broadcast_to((jnp.arange(device_count) % N_INST).astype(jnp.int32)[:, None], (device_count, SURF))
    modal_grad = jnp.zeros((N_INST, MODES, RHS), jnp.float32).at[inst_of, modes_dev].add(terms)
    return psi_now, modal_grad
```

```python
import math

import jax
import jax.numpy as jnp
import numpy as np
from jax import lax
from jax.sharding import Mesh
from jax.sharding import PartitionSpec as P

ITERS = 6
INST_ROWS = 4


def ring(count, shift):
    return [(i, (i + shift) % count) for i in range(count)]


def loop_weight(offset, inst_count):
    angle = math.pi * offset / inst_count
    parity = jnp.cos(math.pi * offset)
    sine_safe = jnp.where(offset == 0, 1.0, jnp.sin(angle))
    value = 0.5 * parity / sine_safe
    return jnp.where(offset == 0, 0.0, value)


def block_sweep(blocks, block_cols, jacobians, row_table):
    picked = blocks[block_cols]
    products = jnp.einsum("nrk,nkl->nrl", picked, jacobians, preferred_element_type=jnp.float32)
    return jnp.einsum("nrl,nb->brl", products, row_table, precision=lax.Precision.HIGHEST)


def face_exchange(psi_b, face_map, face_blocks):
    n_blk = lax.axis_size("blk")
    n_span = lax.axis_size("span")
    head = psi_b[:face_blocks]
    tail = psi_b[-face_blocks:]
    if n_blk == 2:
        both = lax.ppermute(jnp.concatenate([tail, head], axis=0), "blk", ring(2, 1))
        passage = both
    else:
        prev_face = lax.ppermute(tail, "blk", ring(n_blk, 1))
        next_face = lax.ppermute(head, "blk", ring(n_blk, -1))
        passage = jnp.concatenate([prev_face, next_face], axis=0)
    passage = passage[face_map]
    lower = lax.ppermute(tail, "span", [(i, i + 1) for i in range(n_span - 1)])
    upper = lax.ppermute(head, "span", [(i + 1, i) for i in range(n_span - 1)])
    return jnp.concatenate([passage, lower, upper], axis=0)


def spectral_half(half, first_axis, second_axis, weight_of):
    n1 = lax.axis_size(first_axis)
    n2 = lax.axis_size(second_axis)
    gathered = [half.astype(jnp.float32)] + [
        lax.ppermute(half, first_axis, ring(n1, k)).astype(jnp.float32) for k in range(1, n1)
    ]
    own = None
    received = []
    for k2 in range(n2):
        part = None
        for k in range(n1):
            term = weight_of(k, k2) * gathered[k]
            part = term if part is None else part + term
        if k2 == 0:
            own = part
        else:
            received.append(lax.ppermute(part.astype(jnp.bfloat16), second_axis, ring(n2, k2)))
    total = own
    for r in received:
        total = total + r.astype(jnp.float32)
    return total


def on_device(
    source,
    jac_interior,
    interior_rows,
    interior_cols,
    jac_face,
    face_rows,
    face_cols,
    face_map,
    frequency,
    surf_mode,
    surf_row,
    surf_node,
    mode_shape,
):
    objectives = source.shape[1]
    columns = source.shape[2]
    block_rows = jac_interior.shape[2]
    num_blocks = columns // block_rows
    face_blocks = face_map.shape[0] // 2
    nz = lax.axis_size("iz")
    ny = lax.axis_size("iy")
    inst_count = nz * ny
    iz = lax.axis_index("iz")
    iy = lax.axis_index("iy")
    inner_table = jax.nn.one_hot(interior_rows[0], num_blocks, dtype=jnp.float32)
    outer_table = jax.nn.one_hot(face_rows[0], num_blocks, dtype=jnp.float32)
    inner_jac = jac_interior[0]
    outer_jac = jac_face[0]
    inner_cols = interior_cols[0]
    outer_cols = face_cols[0]
    step_rate = frequency[0]
    mode_full = lax.all_gather(mode_shape, "blk", axis=0, tiled=True)

    def to_blocks(a):
        return a.reshape(objectives, num_blocks, block_rows).transpose(1, 0, 2)

    source_b = to_blocks(source[0])
    source_wide = source_b.astype(jnp.float32)

    def w_a(k, k2):
        j = ((iz - k) % nz) * ny + iy
        i = iz * ny + (iy + k2) % ny
        return loop_weight((j - i).astype(jnp.float32), inst_count)

    def w_b(k, k2):
        j = iz * ny + (iy - k) % ny
        i = ((iz + k2) % nz) * ny + iy
        return loop_weight((j - i).astype(jnp.float32), inst_count)

    half_at = num_blocks // 2
    psi_b = source_b
    for sweep_step in range(ITERS):
        face_sources = face_exchange(psi_b, face_map, face_blocks)
        spec_a = spectral_half(psi_b[:half_at], "iz", "iy", w_a)
        spec_b = spectral_half(psi_b[half_at:], "iy", "iz", w_b)
        inner_sum = block_sweep(psi_b, inner_cols, inner_jac, inner_table)
        outer_sum = block_sweep(face_sources, outer_cols, outer_jac, outer_table)
        spectral = jnp.concatenate([spec_a, spec_b], axis=0)
        psi_b = (source_wide - inner_sum - outer_sum - step_rate * spectral).astype(jnp.bfloat16)
    psi_now = psi_b.transpose(1, 0, 2).reshape(objectives, columns)
    loads = psi_now[:, surf_row[0]].astype(jnp.float32)
    entry_modes = surf_mode[:, 0]
    entry_nodes = surf_node[0]
    total_modes = mode_full.shape[0]
    shape_vals = mode_full[entry_modes, entry_nodes]
    mode_table = (entry_modes[:, None] == jnp.arange(total_modes)[None, :]).astype(jnp.float32)
    owner_table = mode_table * shape_vals[:, None]
    contrib = jnp.einsum("re,em->mr", loads, owner_table, precision=lax.Precision.HIGHEST)
    contrib = lax.psum(contrib, ("blk", "span"))
    mode_dev = mode_shape.shape[0]
    own_modes = lax.dynamic_slice_in_dim(contrib, lax.axis_index("blk") * mode_dev, mode_dev, axis=0)
    return (psi_now[None], own_modes[None])


def solution(mesh):
    n_blk, n_span, n_inst = (mesh.shape[a] for a in ("blk", "span", "inst"))
    rows = INST_ROWS if n_inst % INST_ROWS == 0 else 1
    devices = np.asarray(mesh.devices).reshape(n_blk, n_span, rows, n_inst // rows)
    grid = Mesh(devices, ("blk", "span", "iz", "iy"))
    inst = ("iz", "iy")
    dev = ("blk", "span", "iz", "iy")
    return jax.shard_map(
        on_device,
        mesh=grid,
        in_specs=(
            P(inst, None, ("blk", "span")),
            P(dev, None, None, None),
            P(dev, None),
            P(dev, None),
            P(dev, None, None, None),
            P(dev, None),
            P(dev, None),
            P(),
            P(),
            P(dev, None),
            P(dev, None),
            P(dev, None),
            P("blk", None),
        ),
        out_specs=(P(inst, None, ("blk", "span")), P(inst, "blk", None)),
        check_vma=False,
    )
```

```python
import math

import jax
import jax.numpy as jnp
import numpy as np
from jax import lax
from jax.experimental import pallas as pl
from jax.experimental.pallas import tpu as pltpu
from jax.sharding import Mesh
from jax.sharding import PartitionSpec as P

ITERS = 6
INST_ROWS = 4


def ring(count, shift):
    return [(i, (i + shift) % count) for i in range(count)]


def loop_weight(offset, inst_count):
    angle = math.pi * offset / inst_count
    parity = jnp.cos(math.pi * offset)
    sine_safe = jnp.where(offset == 0, 1.0, jnp.sin(angle))
    value = 0.5 * parity / sine_safe
    return jnp.where(offset == 0, 0.0, value)


def block_sweep(blocks, block_cols, jacobians, row_table):
    picked = blocks[block_cols]
    products = jnp.einsum("nrk,nkl->nrl", picked, jacobians, preferred_element_type=jnp.float32)
    return jnp.einsum("nrl,nb->brl", products, row_table, precision=lax.Precision.HIGHEST)


def local_kernel(rows_ref, cols_ref, src_ref, jac_ref, out_ref):
    n = pl.program_id(0)

    @pl.when(n == 0)
    def _():
        out_ref[...] = jnp.zeros_like(out_ref)

    product = jnp.dot(src_ref[0], jac_ref[0], preferred_element_type=jnp.float32)
    row = rows_ref[n]
    out_ref[row] = out_ref[row] + product


def local_sweep(rows_all, cols_all, blocks, jac_all, num_blocks, interpret=False):
    count, objectives, block_rows = jac_all.shape[0], blocks.shape[1], blocks.shape[2]
    return pl.pallas_call(
        local_kernel,
        grid_spec=pltpu.PrefetchScalarGridSpec(
            num_scalar_prefetch=2,
            grid=(count,),
            in_specs=[
                pl.BlockSpec((1, objectives, block_rows), lambda n, rows, cols: (cols[n], 0, 0)),
                pl.BlockSpec((1, block_rows, block_rows), lambda n, rows, cols: (n, 0, 0)),
            ],
            out_specs=pl.BlockSpec((num_blocks, objectives, block_rows), lambda n, rows, cols: (0, 0, 0)),
        ),
        out_shape=jax.ShapeDtypeStruct((num_blocks, objectives, block_rows), jnp.float32),
        interpret=interpret,
    )(rows_all, cols_all, blocks, jac_all)


def face_exchange(psi_b, face_blocks):
    n_blk = lax.axis_size("blk")
    n_span = lax.axis_size("span")
    head = psi_b[:face_blocks]
    tail = psi_b[-face_blocks:]
    if n_blk == 2:
        passage = lax.ppermute(jnp.concatenate([tail, head], axis=0), "blk", ring(2, 1))
    else:
        prev_face = lax.ppermute(tail, "blk", ring(n_blk, 1))
        next_face = lax.ppermute(head, "blk", ring(n_blk, -1))
        passage = jnp.concatenate([prev_face, next_face], axis=0)
    lower = lax.ppermute(tail, "span", [(i, i + 1) for i in range(n_span - 1)])
    upper = lax.ppermute(head, "span", [(i + 1, i) for i in range(n_span - 1)])
    return jnp.concatenate([passage, lower, upper], axis=0)


def ordered_sum(value, axis):
    count = lax.axis_size(axis)
    me = lax.axis_index(axis)
    slots = [None] * count
    pieces = [value] + [lax.ppermute(value, axis, ring(count, k)) for k in range(1, count)]
    for place in range(count):
        pick = jnp.zeros_like(value)
        for k in range(count):
            pick = jnp.where((me - k) % count == place, pieces[k], pick)
        slots[place] = pick
    while len(slots) > 1:
        slots = [slots[i] + slots[i + 1] if i + 1 < len(slots) else slots[i] for i in range(0, len(slots), 2)]
    return slots[0]


def spectral_half(half, first_axis, second_axis, weight_of):
    n1 = lax.axis_size(first_axis)
    n2 = lax.axis_size(second_axis)
    gathered = [half.astype(jnp.float32)] + [
        lax.ppermute(half, first_axis, ring(n1, k)).astype(jnp.float32) for k in range(1, n1)
    ]
    own = None
    received = []
    for k2 in range(n2):
        part = None
        for k in range(n1):
            term = weight_of(k, k2) * gathered[k]
            part = term if part is None else part + term
        if k2 == 0:
            own = part
        else:
            received.append(lax.ppermute(part.astype(jnp.bfloat16), second_axis, ring(n2, k2)))
    total = own
    for r in received:
        total = total + r.astype(jnp.float32)
    return total


def on_device(
    source,
    jac_interior,
    interior_rows,
    interior_cols,
    jac_face,
    face_rows,
    face_cols,
    face_map,
    frequency,
    surf_mode,
    surf_row,
    surf_node,
    mode_shape,
):
    objectives = source.shape[1]
    columns = source.shape[2]
    block_rows = jac_interior.shape[2]
    num_blocks = columns // block_rows
    face_blocks = face_map.shape[0] // 2
    nz = lax.axis_size("iz")
    ny = lax.axis_size("iy")
    inst_count = nz * ny
    iz = lax.axis_index("iz")
    iy = lax.axis_index("iy")
    jac_all = jnp.concatenate([jac_interior[0], jac_face[0]], axis=0)
    rows_all = jnp.clip(jnp.concatenate([interior_rows[0], face_rows[0]]), 0, num_blocks - 1)
    face_count = jac_face.shape[1]
    passage_count = face_map.shape[0]
    outer_cols = jnp.clip(face_cols[0], 0, face_count - 1)
    mapped = jnp.clip(face_map[jnp.clip(outer_cols, 0, passage_count - 1)], 0, passage_count - 1)
    face_src = jnp.where(outer_cols < passage_count, mapped, outer_cols)
    cols_all = jnp.concatenate([jnp.clip(interior_cols[0], 0, num_blocks - 1), num_blocks + face_src])
    step_rate = frequency[0]
    mode_full = lax.all_gather(mode_shape, "blk", axis=0, tiled=True)

    def to_blocks(a):
        return a.reshape(objectives, num_blocks, block_rows).transpose(1, 0, 2)

    source_b = to_blocks(source[0])
    source_wide = source_b.astype(jnp.float32)

    def w_a(k, k2):
        j = ((iz - k) % nz) * ny + iy
        i = iz * ny + (iy + k2) % ny
        return loop_weight((j - i).astype(jnp.float32), inst_count)

    def w_b(k, k2):
        j = iz * ny + (iy - k) % ny
        i = ((iz + k2) % nz) * ny + iy
        return loop_weight((j - i).astype(jnp.float32), inst_count)

    half_at = num_blocks // 2
    psi_b = source_b
    for sweep_step in range(ITERS):
        face_raw = face_exchange(psi_b, face_blocks)
        spec_a = spectral_half(psi_b[:half_at], "iz", "iy", w_a)
        spec_b = spectral_half(psi_b[half_at:], "iy", "iz", w_b)
        local = local_sweep(rows_all, cols_all, jnp.concatenate([psi_b, face_raw], axis=0), jac_all, num_blocks)
        spectral = jnp.concatenate([spec_a, spec_b], axis=0)
        psi_b = (source_wide - local - step_rate * spectral).astype(jnp.bfloat16)
    psi_now = psi_b.transpose(1, 0, 2).reshape(objectives, columns)
    loads = psi_now[:, surf_row[0]].astype(jnp.float32)
    entry_modes = surf_mode[:, 0]
    entry_nodes = surf_node[0]
    total_modes = mode_full.shape[0]
    shape_vals = mode_full[entry_modes, entry_nodes]
    mode_table = (entry_modes[:, None] == jnp.arange(total_modes)[None, :]).astype(jnp.float32)
    owner_table = mode_table * shape_vals[:, None]
    contrib = jnp.einsum("re,em->mr", loads, owner_table, precision=lax.Precision.HIGHEST)
    contrib = ordered_sum(ordered_sum(contrib, "blk"), "span")
    mode_dev = mode_shape.shape[0]
    own_modes = lax.dynamic_slice_in_dim(contrib, lax.axis_index("blk") * mode_dev, mode_dev, axis=0)
    return (psi_now[None], own_modes[None])


def solution(mesh):
    n_blk, n_span, n_inst = (mesh.shape[a] for a in ("blk", "span", "inst"))
    rows = INST_ROWS if n_inst % INST_ROWS == 0 else 1
    devices = np.asarray(mesh.devices).reshape(n_blk, n_span, rows, n_inst // rows)
    grid = Mesh(devices, ("blk", "span", "iz", "iy"))
    inst = ("iz", "iy")
    dev = ("blk", "span", "iz", "iy")
    return jax.shard_map(
        on_device,
        mesh=grid,
        in_specs=(
            P(inst, None, ("blk", "span")),
            P(dev, None, None, None),
            P(dev, None),
            P(dev, None),
            P(dev, None, None, None),
            P(dev, None),
            P(dev, None),
            P(),
            P(),
            P(dev, None),
            P(dev, None),
            P(dev, None),
            P("blk", None),
        ),
        out_specs=(P(inst, None, ("blk", "span")), P(inst, "blk", None)),
        check_vma=False,
    )
```

```python
import math

import jax
import jax.numpy as jnp
import numpy as np
from jax import lax
from jax.experimental import pallas as pl
from jax.experimental.pallas import tpu as pltpu
from jax.sharding import Mesh
from jax.sharding import PartitionSpec as P

ITERS = 6
INST_ROWS = 4


def ring(count, shift):
    return [(i, (i + shift) % count) for i in range(count)]


def loop_weight(offset, inst_count):
    angle = math.pi * offset / inst_count
    parity = jnp.cos(math.pi * offset)
    sine_safe = jnp.where(offset == 0, 1.0, jnp.sin(angle))
    value = 0.5 * parity / sine_safe
    return jnp.where(offset == 0, 0.0, value)


def block_sweep(blocks, block_cols, jacobians, row_table):
    picked = blocks[block_cols]
    products = jnp.einsum("nrk,nkl->nrl", picked, jacobians, preferred_element_type=jnp.float32)
    return jnp.einsum("nrl,nb->brl", products, row_table, precision=lax.Precision.HIGHEST)


def local_kernel(rows_ref, cols_ref, psi_ref, face_ref, jac_ref, out_ref):
    n = pl.program_id(0)
    group = jac_ref.shape[0]
    num_blocks = psi_ref.shape[0]
    face_count = face_ref.shape[0]

    @pl.when(n == 0)
    def _():
        out_ref[...] = jnp.zeros_like(out_ref)

    for g in range(group):
        at = n * group + g
        col = cols_ref[at]
        own = psi_ref[jnp.clip(col, 0, num_blocks - 1)]
        face = face_ref[jnp.clip(col - num_blocks, 0, face_count - 1)]
        picked = jnp.where(col < num_blocks, own, face)
        product = jnp.dot(picked, jac_ref[g], preferred_element_type=jnp.float32)
        row = rows_ref[at]
        out_ref[row] = out_ref[row] + product


def local_sweep(rows_all, cols_all, blocks, faces, jac_all, group=6, interpret=False):
    count, block_rows = jac_all.shape[0], jac_all.shape[1]
    num_blocks, objectives = blocks.shape[0], blocks.shape[1]
    face_count = faces.shape[0]
    return pl.pallas_call(
        local_kernel,
        grid_spec=pltpu.PrefetchScalarGridSpec(
            num_scalar_prefetch=2,
            grid=(count // group,),
            in_specs=[
                pl.BlockSpec((num_blocks, objectives, block_rows), lambda n, rows, cols: (0, 0, 0)),
                pl.BlockSpec((face_count, objectives, block_rows), lambda n, rows, cols: (0, 0, 0)),
                pl.BlockSpec((group, block_rows, block_rows), lambda n, rows, cols: (n, 0, 0)),
            ],
            out_specs=pl.BlockSpec((num_blocks, objectives, block_rows), lambda n, rows, cols: (0, 0, 0)),
        ),
        out_shape=jax.ShapeDtypeStruct((num_blocks, objectives, block_rows), jnp.float32),
        interpret=interpret,
    )(rows_all, cols_all, blocks, faces, jac_all)


def face_exchange(psi_b, face_blocks):
    n_blk = lax.axis_size("blk")
    n_span = lax.axis_size("span")
    head = psi_b[:face_blocks]
    tail = psi_b[-face_blocks:]
    if n_blk == 2:
        passage = lax.ppermute(jnp.concatenate([tail, head], axis=0), "blk", ring(2, 1))
    else:
        prev_face = lax.ppermute(tail, "blk", ring(n_blk, 1))
        next_face = lax.ppermute(head, "blk", ring(n_blk, -1))
        passage = jnp.concatenate([prev_face, next_face], axis=0)
    lower = lax.ppermute(tail, "span", [(i, i + 1) for i in range(n_span - 1)])
    upper = lax.ppermute(head, "span", [(i + 1, i) for i in range(n_span - 1)])
    return jnp.concatenate([passage, lower, upper], axis=0)


def ordered_sum(value, axis):
    count = lax.axis_size(axis)
    me = lax.axis_index(axis)
    slots = [None] * count
    pieces = [value] + [lax.ppermute(value, axis, ring(count, k)) for k in range(1, count)]
    for place in range(count):
        pick = jnp.zeros_like(value)
        for k in range(count):
            pick = jnp.where((me - k) % count == place, pieces[k], pick)
        slots[place] = pick
    while len(slots) > 1:
        slots = [slots[i] + slots[i + 1] if i + 1 < len(slots) else slots[i] for i in range(0, len(slots), 2)]
    return slots[0]


def spectral_half(half, first_axis, second_axis, weight_of):
    n1 = lax.axis_size(first_axis)
    n2 = lax.axis_size(second_axis)
    gathered = [half.astype(jnp.float32)] + [
        lax.ppermute(half, first_axis, ring(n1, k)).astype(jnp.float32) for k in range(1, n1)
    ]
    own = None
    received = []
    for k2 in range(n2):
        part = None
        for k in range(n1):
            term = weight_of(k, k2) * gathered[k]
            part = term if part is None else part + term
        if k2 == 0:
            own = part
        else:
            received.append(lax.ppermute(part.astype(jnp.bfloat16), second_axis, ring(n2, k2)))
    total = own
    for r in received:
        total = total + r.astype(jnp.float32)
    return total


def on_device(
    source,
    jac_interior,
    interior_rows,
    interior_cols,
    jac_face,
    face_rows,
    face_cols,
    face_map,
    frequency,
    surf_mode,
    surf_row,
    surf_node,
    mode_shape,
):
    objectives = source.shape[1]
    columns = source.shape[2]
    block_rows = jac_interior.shape[2]
    num_blocks = columns // block_rows
    face_blocks = face_map.shape[0] // 2
    nz = lax.axis_size("iz")
    ny = lax.axis_size("iy")
    inst_count = nz * ny
    iz = lax.axis_index("iz")
    iy = lax.axis_index("iy")
    jac_all = jnp.concatenate([jac_interior[0], jac_face[0]], axis=0)
    rows_all = jnp.clip(jnp.concatenate([interior_rows[0], face_rows[0]]), 0, num_blocks - 1)
    face_count = jac_face.shape[1]
    passage_count = face_map.shape[0]
    outer_cols = jnp.clip(face_cols[0], 0, face_count - 1)
    mapped = jnp.clip(face_map[jnp.clip(outer_cols, 0, passage_count - 1)], 0, passage_count - 1)
    face_src = jnp.where(outer_cols < passage_count, mapped, outer_cols)
    cols_all = jnp.concatenate([jnp.clip(interior_cols[0], 0, num_blocks - 1), num_blocks + face_src])
    step_rate = frequency[0]
    mode_full = lax.all_gather(mode_shape, "blk", axis=0, tiled=True)

    def to_blocks(a):
        return a.reshape(objectives, num_blocks, block_rows).transpose(1, 0, 2)

    source_b = to_blocks(source[0])
    source_wide = source_b.astype(jnp.float32)

    def w_a(k, k2):
        j = ((iz - k) % nz) * ny + iy
        i = iz * ny + (iy + k2) % ny
        return loop_weight((j - i).astype(jnp.float32), inst_count)

    def w_b(k, k2):
        j = iz * ny + (iy - k) % ny
        i = ((iz + k2) % nz) * ny + iy
        return loop_weight((j - i).astype(jnp.float32), inst_count)

    half_at = num_blocks // 2
    psi_b = source_b
    for sweep_step in range(ITERS):
        face_raw = face_exchange(psi_b, face_blocks)
        spec_a = spectral_half(psi_b[:half_at], "iz", "iy", w_a)
        spec_b = spectral_half(psi_b[half_at:], "iy", "iz", w_b)
        local = local_sweep(rows_all, cols_all, psi_b, face_raw, jac_all)
        spectral = jnp.concatenate([spec_a, spec_b], axis=0)
        psi_b = (source_wide - local - step_rate * spectral).astype(jnp.bfloat16)
    psi_now = psi_b.transpose(1, 0, 2).reshape(objectives, columns)
    loads = psi_now[:, surf_row[0]].astype(jnp.float32)
    entry_modes = surf_mode[:, 0]
    entry_nodes = surf_node[0]
    total_modes = mode_full.shape[0]
    shape_vals = mode_full[entry_modes, entry_nodes]
    mode_table = (entry_modes[:, None] == jnp.arange(total_modes)[None, :]).astype(jnp.float32)
    owner_table = mode_table * shape_vals[:, None]
    contrib = jnp.einsum("re,em->mr", loads, owner_table, precision=lax.Precision.HIGHEST)
    contrib = ordered_sum(ordered_sum(contrib, "blk"), "span")
    mode_dev = mode_shape.shape[0]
    own_modes = lax.dynamic_slice_in_dim(contrib, lax.axis_index("blk") * mode_dev, mode_dev, axis=0)
    return (psi_now[None], own_modes[None])


def solution(mesh):
    n_blk, n_span, n_inst = (mesh.shape[a] for a in ("blk", "span", "inst"))
    rows = INST_ROWS if n_inst % INST_ROWS == 0 else 1
    devices = np.asarray(mesh.devices).reshape(n_blk, n_span, rows, n_inst // rows)
    grid = Mesh(devices, ("blk", "span", "iz", "iy"))
    inst = ("iz", "iy")
    dev = ("blk", "span", "iz", "iy")
    return jax.shard_map(
        on_device,
        mesh=grid,
        in_specs=(
            P(inst, None, ("blk", "span")),
            P(dev, None, None, None),
            P(dev, None),
            P(dev, None),
            P(dev, None, None, None),
            P(dev, None),
            P(dev, None),
            P(),
            P(),
            P(dev, None),
            P(dev, None),
            P(dev, None),
            P("blk", None),
        ),
        out_specs=(P(inst, None, ("blk", "span")), P(inst, "blk", None)),
        check_vma=False,
    )
```

```python
import math

import jax
import jax.numpy as jnp
import numpy as np
from jax import lax
from jax.experimental import pallas as pl
from jax.experimental.pallas import tpu as pltpu
from jax.sharding import Mesh
from jax.sharding import PartitionSpec as P

ITERS = 6
INST_ROWS = 4


def ring(count, shift):
    return [(i, (i + shift) % count) for i in range(count)]


def loop_weight(offset, inst_count):
    angle = math.pi * offset / inst_count
    parity = jnp.cos(math.pi * offset)
    sine_safe = jnp.where(offset == 0, 1.0, jnp.sin(angle))
    value = 0.5 * parity / sine_safe
    return jnp.where(offset == 0, 0.0, value)


def block_sweep(blocks, block_cols, jacobians, row_table):
    picked = blocks[block_cols]
    products = jnp.einsum("nrk,nkl->nrl", picked, jacobians, preferred_element_type=jnp.float32)
    return jnp.einsum("nrl,nb->brl", products, row_table, precision=lax.Precision.HIGHEST)


def local_kernel(rows_ref, cols_ref, psi_ref, face_ref, jac_ref, out_ref):
    n = pl.program_id(0)
    group = jac_ref.shape[0]
    num_blocks = psi_ref.shape[0]
    face_count = face_ref.shape[0]

    @pl.when(n == 0)
    def _():
        out_ref[...] = jnp.zeros_like(out_ref)

    for g in range(group):
        at = n * group + g
        col = cols_ref[at]
        own = psi_ref[jnp.clip(col, 0, num_blocks - 1)]
        face = face_ref[jnp.clip(col - num_blocks, 0, face_count - 1)]
        picked = jnp.where(col < num_blocks, own, face)
        product = jnp.dot(picked, jac_ref[g], preferred_element_type=jnp.float32)
        row = rows_ref[at]
        out_ref[row] = out_ref[row] + product


def local_sweep(rows_all, cols_all, blocks, faces, jac_all, group=6, interpret=False):
    count, block_rows = jac_all.shape[0], jac_all.shape[1]
    num_blocks, objectives = blocks.shape[0], blocks.shape[1]
    face_count = faces.shape[0]
    return pl.pallas_call(
        local_kernel,
        grid_spec=pltpu.PrefetchScalarGridSpec(
            num_scalar_prefetch=2,
            grid=(count // group,),
            in_specs=[
                pl.BlockSpec((num_blocks, objectives, block_rows), lambda n, rows, cols: (0, 0, 0)),
                pl.BlockSpec((face_count, objectives, block_rows), lambda n, rows, cols: (0, 0, 0)),
                pl.BlockSpec((group, block_rows, block_rows), lambda n, rows, cols: (n, 0, 0)),
            ],
            out_specs=pl.BlockSpec((num_blocks, objectives, block_rows), lambda n, rows, cols: (0, 0, 0)),
        ),
        out_shape=jax.ShapeDtypeStruct((num_blocks, objectives, block_rows), jnp.float32),
        interpret=interpret,
    )(rows_all, cols_all, blocks, faces, jac_all)


def face_exchange(psi_b, face_blocks):
    n_blk = lax.axis_size("blk")
    n_span = lax.axis_size("span")
    head = psi_b[:face_blocks]
    tail = psi_b[-face_blocks:]
    if n_blk == 2:
        passage = lax.ppermute(jnp.concatenate([tail, head], axis=0), "blk", ring(2, 1))
    else:
        prev_face = lax.ppermute(tail, "blk", ring(n_blk, 1))
        next_face = lax.ppermute(head, "blk", ring(n_blk, -1))
        passage = jnp.concatenate([prev_face, next_face], axis=0)
    lower = lax.ppermute(tail, "span", [(i, i + 1) for i in range(n_span - 1)])
    upper = lax.ppermute(head, "span", [(i + 1, i) for i in range(n_span - 1)])
    return jnp.concatenate([passage, lower, upper], axis=0)


def ordered_sum(value, axis):
    count = lax.axis_size(axis)
    me = lax.axis_index(axis)
    slots = [None] * count
    pieces = [value] + [lax.ppermute(value, axis, ring(count, k)) for k in range(1, count)]
    for place in range(count):
        pick = jnp.zeros_like(value)
        for k in range(count):
            pick = jnp.where((me - k) % count == place, pieces[k], pick)
        slots[place] = pick
    while len(slots) > 1:
        slots = [slots[i] + slots[i + 1] if i + 1 < len(slots) else slots[i] for i in range(0, len(slots), 2)]
    return slots[0]


def gather_half(half, first_axis):
    n1 = lax.axis_size(first_axis)
    return [half] + [lax.ppermute(half, first_axis, ring(n1, k)) for k in range(1, n1)]


def spread_half(gathered, second_axis, weight_of):
    n1 = len(gathered)
    n2 = lax.axis_size(second_axis)
    wide = [g.astype(jnp.float32) for g in gathered]
    own = None
    received = []
    for k2 in range(n2):
        part = None
        for k in range(n1):
            term = weight_of(k, k2) * wide[k]
            part = term if part is None else part + term
        if k2 == 0:
            own = part
        else:
            received.append(lax.ppermute(part.astype(jnp.bfloat16), second_axis, ring(n2, k2)))
    total = own
    for r in received:
        total = total + r.astype(jnp.float32)
    return total


def on_device(
    source,
    jac_interior,
    interior_rows,
    interior_cols,
    jac_face,
    face_rows,
    face_cols,
    face_map,
    frequency,
    surf_mode,
    surf_row,
    surf_node,
    mode_shape,
):
    objectives = source.shape[1]
    columns = source.shape[2]
    block_rows = jac_interior.shape[2]
    num_blocks = columns // block_rows
    face_blocks = face_map.shape[0] // 2
    nz = lax.axis_size("iz")
    ny = lax.axis_size("iy")
    inst_count = nz * ny
    iz = lax.axis_index("iz")
    iy = lax.axis_index("iy")
    jac_all = jnp.concatenate([jac_interior[0], jac_face[0]], axis=0)
    rows_all = jnp.clip(jnp.concatenate([interior_rows[0], face_rows[0]]), 0, num_blocks - 1)
    face_count = jac_face.shape[1]
    passage_count = face_map.shape[0]
    outer_cols = jnp.clip(face_cols[0], 0, face_count - 1)
    mapped = jnp.clip(face_map[jnp.clip(outer_cols, 0, passage_count - 1)], 0, passage_count - 1)
    face_src = jnp.where(outer_cols < passage_count, mapped, outer_cols)
    cols_all = jnp.concatenate([jnp.clip(interior_cols[0], 0, num_blocks - 1), num_blocks + face_src])
    step_rate = frequency[0]
    mode_full = lax.all_gather(mode_shape, "blk", axis=0, tiled=True)

    def to_blocks(a):
        return a.reshape(objectives, num_blocks, block_rows).transpose(1, 0, 2)

    source_b = to_blocks(source[0])
    source_wide = source_b.astype(jnp.float32)

    def w_a(k, k2):
        j = ((iz - k) % nz) * ny + iy
        i = iz * ny + (iy + k2) % ny
        return loop_weight((j - i).astype(jnp.float32), inst_count)

    def w_b(k, k2):
        j = iz * ny + (iy - k) % ny
        i = ((iz + k2) % nz) * ny + iy
        return loop_weight((j - i).astype(jnp.float32), inst_count)

    half_at = num_blocks // 2
    psi_b = source_b
    for sweep_step in range(ITERS):
        face_raw = face_exchange(psi_b, face_blocks)
        got_a = gather_half(psi_b[:half_at], "iz")
        got_b = gather_half(psi_b[half_at:], "iy")
        local = local_sweep(rows_all, cols_all, psi_b, face_raw, jac_all)
        got_a, got_b, local = lax.optimization_barrier((got_a, got_b, local))
        spec_a = spread_half(got_a, "iy", w_a)
        spec_b = spread_half(got_b, "iz", w_b)
        spectral = jnp.concatenate([spec_a, spec_b], axis=0)
        psi_b = (source_wide - local - step_rate * spectral).astype(jnp.bfloat16)
    psi_now = psi_b.transpose(1, 0, 2).reshape(objectives, columns)
    loads = psi_now[:, surf_row[0]].astype(jnp.float32)
    entry_modes = surf_mode[:, 0]
    entry_nodes = surf_node[0]
    total_modes = mode_full.shape[0]
    shape_vals = mode_full[entry_modes, entry_nodes]
    mode_table = (entry_modes[:, None] == jnp.arange(total_modes)[None, :]).astype(jnp.float32)
    owner_table = mode_table * shape_vals[:, None]
    contrib = jnp.einsum("re,em->mr", loads, owner_table, precision=lax.Precision.HIGHEST)
    contrib = ordered_sum(ordered_sum(contrib, "blk"), "span")
    mode_dev = mode_shape.shape[0]
    own_modes = lax.dynamic_slice_in_dim(contrib, lax.axis_index("blk") * mode_dev, mode_dev, axis=0)
    return (psi_now[None], own_modes[None])


def solution(mesh):
    n_blk, n_span, n_inst = (mesh.shape[a] for a in ("blk", "span", "inst"))
    rows = INST_ROWS if n_inst % INST_ROWS == 0 else 1
    devices = np.asarray(mesh.devices).reshape(n_blk, n_span, rows, n_inst // rows)
    grid = Mesh(devices, ("blk", "span", "iz", "iy"))
    inst = ("iz", "iy")
    dev = ("blk", "span", "iz", "iy")
    return jax.shard_map(
        on_device,
        mesh=grid,
        in_specs=(
            P(inst, None, ("blk", "span")),
            P(dev, None, None, None),
            P(dev, None),
            P(dev, None),
            P(dev, None, None, None),
            P(dev, None),
            P(dev, None),
            P(),
            P(),
            P(dev, None),
            P(dev, None),
            P(dev, None),
            P("blk", None),
        ),
        out_specs=(P(inst, None, ("blk", "span")), P(inst, "blk", None)),
        check_vma=False,
    )
```

```python
import math

import jax
import jax.numpy as jnp
import numpy as np
from jax import lax
from jax.experimental import pallas as pl
from jax.experimental.pallas import tpu as pltpu
from jax.sharding import Mesh
from jax.sharding import PartitionSpec as P

ITERS = 6
INST_ROWS = 4


def ring(count, shift):
    return [(i, (i + shift) % count) for i in range(count)]


def loop_weight(offset, inst_count):
    angle = math.pi * offset / inst_count
    parity = jnp.cos(math.pi * offset)
    sine_safe = jnp.where(offset == 0, 1.0, jnp.sin(angle))
    value = 0.5 * parity / sine_safe
    return jnp.where(offset == 0, 0.0, value)


def block_sweep(blocks, block_cols, jacobians, row_table):
    picked = blocks[block_cols]
    products = jnp.einsum("nrk,nkl->nrl", picked, jacobians, preferred_element_type=jnp.float32)
    return jnp.einsum("nrl,nb->brl", products, row_table, precision=lax.Precision.HIGHEST)


def local_kernel(rows_ref, cols_ref, psi_ref, face_ref, jac_ref, out_ref):
    n = pl.program_id(0)
    group = jac_ref.shape[0]
    num_blocks = psi_ref.shape[0]
    face_count = face_ref.shape[0]

    @pl.when(n == 0)
    def _():
        out_ref[...] = jnp.zeros_like(out_ref)

    for g in range(group):
        at = n * group + g
        col = cols_ref[at]
        own = psi_ref[jnp.clip(col, 0, num_blocks - 1)]
        face = face_ref[jnp.clip(col - num_blocks, 0, face_count - 1)]
        picked = jnp.where(col < num_blocks, own, face)
        product = jnp.dot(picked, jac_ref[g], preferred_element_type=jnp.float32)
        row = rows_ref[at]
        out_ref[row] = out_ref[row] + product


def local_sweep(rows_all, cols_all, blocks, faces, jac_all, group=6, interpret=False):
    count, block_rows = jac_all.shape[0], jac_all.shape[1]
    num_blocks, objectives = blocks.shape[0], blocks.shape[1]
    face_count = faces.shape[0]
    return pl.pallas_call(
        local_kernel,
        grid_spec=pltpu.PrefetchScalarGridSpec(
            num_scalar_prefetch=2,
            grid=(count // group,),
            in_specs=[
                pl.BlockSpec((num_blocks, objectives, block_rows), lambda n, rows, cols: (0, 0, 0)),
                pl.BlockSpec((face_count, objectives, block_rows), lambda n, rows, cols: (0, 0, 0)),
                pl.BlockSpec((group, block_rows, block_rows), lambda n, rows, cols: (n, 0, 0)),
            ],
            out_specs=pl.BlockSpec((num_blocks, objectives, block_rows), lambda n, rows, cols: (0, 0, 0)),
        ),
        out_shape=jax.ShapeDtypeStruct((num_blocks, objectives, block_rows), jnp.float32),
        interpret=interpret,
    )(rows_all, cols_all, blocks, faces, jac_all)


def face_exchange(psi_b, face_blocks):
    n_blk = lax.axis_size("blk")
    n_span = lax.axis_size("span")
    head = psi_b[:face_blocks]
    tail = psi_b[-face_blocks:]
    if n_blk == 2:
        passage = lax.ppermute(jnp.concatenate([tail, head], axis=0), "blk", ring(2, 1))
    else:
        prev_face = lax.ppermute(tail, "blk", ring(n_blk, 1))
        next_face = lax.ppermute(head, "blk", ring(n_blk, -1))
        passage = jnp.concatenate([prev_face, next_face], axis=0)
    lower = lax.ppermute(tail, "span", [(i, i + 1) for i in range(n_span - 1)])
    upper = lax.ppermute(head, "span", [(i + 1, i) for i in range(n_span - 1)])
    return jnp.concatenate([passage, lower, upper], axis=0)


def ordered_sum(value, axis):
    count = lax.axis_size(axis)
    me = lax.axis_index(axis)
    slots = [None] * count
    pieces = [value] + [lax.ppermute(value, axis, ring(count, k)) for k in range(1, count)]
    for place in range(count):
        pick = jnp.zeros_like(value)
        for k in range(count):
            pick = jnp.where((me - k) % count == place, pieces[k], pick)
        slots[place] = pick
    while len(slots) > 1:
        slots = [slots[i] + slots[i + 1] if i + 1 < len(slots) else slots[i] for i in range(0, len(slots), 2)]
    return slots[0]


def gather_half(half, first_axis):
    n1 = lax.axis_size(first_axis)
    return [half] + [lax.ppermute(half, first_axis, ring(n1, k)) for k in range(1, n1)]


def spread_half(gathered, second_axis, weight_of):
    n1 = len(gathered)
    n2 = lax.axis_size(second_axis)
    wide = [g.astype(jnp.float32) for g in gathered]
    own = None
    received = []
    for k2 in range(n2):
        part = None
        for k in range(n1):
            term = weight_of(k, k2) * wide[k]
            part = term if part is None else part + term
        if k2 == 0:
            own = part
        else:
            received.append(lax.ppermute(part.astype(jnp.bfloat16), second_axis, ring(n2, k2)))
    total = own
    for r in received:
        total = total + r.astype(jnp.float32)
    return total


def on_device(
    source,
    jac_interior,
    interior_rows,
    interior_cols,
    jac_face,
    face_rows,
    face_cols,
    face_map,
    frequency,
    surf_mode,
    surf_row,
    surf_node,
    mode_shape,
):
    objectives = source.shape[1]
    columns = source.shape[2]
    block_rows = jac_interior.shape[2]
    num_blocks = columns // block_rows
    face_blocks = face_map.shape[0] // 2
    nz = lax.axis_size("iz")
    ny = lax.axis_size("iy")
    inst_count = nz * ny
    iz = lax.axis_index("iz")
    iy = lax.axis_index("iy")
    jac_all = jnp.concatenate([jac_interior[0], jac_face[0]], axis=0)
    rows_all = jnp.clip(jnp.concatenate([interior_rows[0], face_rows[0]]), 0, num_blocks - 1)
    face_count = jac_face.shape[1]
    passage_count = face_map.shape[0]
    outer_cols = jnp.clip(face_cols[0], 0, face_count - 1)
    mapped = jnp.clip(face_map[jnp.clip(outer_cols, 0, passage_count - 1)], 0, passage_count - 1)
    face_src = jnp.where(outer_cols < passage_count, mapped, outer_cols)
    cols_all = jnp.concatenate([jnp.clip(interior_cols[0], 0, num_blocks - 1), num_blocks + face_src])
    step_rate = frequency[0]
    mode_full = lax.all_gather(mode_shape, "blk", axis=0, tiled=True)

    def to_blocks(a):
        return a.reshape(objectives, num_blocks, block_rows).transpose(1, 0, 2)

    source_b = to_blocks(source[0])
    source_wide = source_b.astype(jnp.float32)

    def w_a(k, k2):
        j = ((iz - k) % nz) * ny + iy
        i = iz * ny + (iy + k2) % ny
        return loop_weight((j - i).astype(jnp.float32), inst_count)

    def w_b(k, k2):
        j = iz * ny + (iy - k) % ny
        i = ((iz + k2) % nz) * ny + iy
        return loop_weight((j - i).astype(jnp.float32), inst_count)

    half_at = num_blocks // 2
    psi_b = source_b
    for sweep_step in range(ITERS):
        face_raw = face_exchange(psi_b, face_blocks)
        got_a = gather_half(psi_b, "iz")
        local = local_sweep(rows_all, cols_all, psi_b, face_raw, jac_all)
        got_a, local = lax.optimization_barrier((got_a, local))
        spectral = spread_half(got_a, "iy", w_a)
        psi_b = (source_wide - local - step_rate * spectral).astype(jnp.bfloat16)
    psi_now = psi_b.transpose(1, 0, 2).reshape(objectives, columns)
    loads = psi_now[:, surf_row[0]].astype(jnp.float32)
    entry_modes = surf_mode[:, 0]
    entry_nodes = surf_node[0]
    total_modes = mode_full.shape[0]
    shape_vals = mode_full[entry_modes, entry_nodes]
    mode_table = (entry_modes[:, None] == jnp.arange(total_modes)[None, :]).astype(jnp.float32)
    owner_table = mode_table * shape_vals[:, None]
    contrib = jnp.einsum("re,em->mr", loads, owner_table, precision=lax.Precision.HIGHEST)
    contrib = ordered_sum(ordered_sum(contrib, "blk"), "span")
    mode_dev = mode_shape.shape[0]
    own_modes = lax.dynamic_slice_in_dim(contrib, lax.axis_index("blk") * mode_dev, mode_dev, axis=0)
    return (psi_now[None], own_modes[None])


def solution(mesh):
    n_blk, n_span, n_inst = (mesh.shape[a] for a in ("blk", "span", "inst"))
    rows = INST_ROWS if n_inst % INST_ROWS == 0 else 1
    devices = np.asarray(mesh.devices).reshape(n_blk, n_span, rows, n_inst // rows)
    grid = Mesh(devices, ("blk", "span", "iz", "iy"))
    inst = ("iz", "iy")
    dev = ("blk", "span", "iz", "iy")
    return jax.shard_map(
        on_device,
        mesh=grid,
        in_specs=(
            P(inst, None, ("blk", "span")),
            P(dev, None, None, None),
            P(dev, None),
            P(dev, None),
            P(dev, None, None, None),
            P(dev, None),
            P(dev, None),
            P(),
            P(),
            P(dev, None),
            P(dev, None),
            P(dev, None),
            P("blk", None),
        ),
        out_specs=(P(inst, None, ("blk", "span")), P(inst, "blk", None)),
        check_vma=False,
    )
```

```python
import math

import jax
import jax.numpy as jnp
import numpy as np
from jax import lax
from jax.experimental import pallas as pl
from jax.experimental.pallas import tpu as pltpu
from jax.sharding import Mesh
from jax.sharding import PartitionSpec as P

ITERS = 6
INST_ROWS = 4


def ring(count, shift):
    return [(i, (i + shift) % count) for i in range(count)]


def loop_weight(offset, inst_count):
    angle = math.pi * offset / inst_count
    parity = jnp.cos(math.pi * offset)
    sine_safe = jnp.where(offset == 0, 1.0, jnp.sin(angle))
    value = 0.5 * parity / sine_safe
    return jnp.where(offset == 0, 0.0, value)


def block_sweep(blocks, block_cols, jacobians, row_table):
    picked = blocks[block_cols]
    products = jnp.einsum("nrk,nkl->nrl", picked, jacobians, preferred_element_type=jnp.float32)
    return jnp.einsum("nrl,nb->brl", products, row_table, precision=lax.Precision.HIGHEST)


def local_kernel(rows_in, cols_in, rows_out, cols_out, psi_ref, face_ref, jin_ref, jout_ref, out_ref):
    n = pl.program_id(0)

    @pl.when(n == 0)
    def _():
        out_ref[...] = jnp.zeros_like(out_ref)

    for rows, cols, blocks, jac in ((rows_in, cols_in, psi_ref, jin_ref), (rows_out, cols_out, face_ref, jout_ref)):
        group = jac.shape[0]
        for g in range(group):
            at = n * group + g
            product = jnp.dot(blocks[cols[at]], jac[g], preferred_element_type=jnp.float32)
            row = rows[at]
            out_ref[row] = out_ref[row] + product


def local_sweep(tables, blocks, faces, jac_in, jac_out, interpret=False):
    steps = math.gcd(jac_in.shape[0], jac_out.shape[0])
    block_rows = jac_in.shape[1]
    num_blocks, objectives = blocks.shape[0], blocks.shape[1]
    face_count = faces.shape[0]
    whole = lambda n, *refs: (0, 0, 0)
    return pl.pallas_call(
        local_kernel,
        grid_spec=pltpu.PrefetchScalarGridSpec(
            num_scalar_prefetch=4,
            grid=(steps,),
            in_specs=[
                pl.BlockSpec((num_blocks, objectives, block_rows), whole),
                pl.BlockSpec((face_count, objectives, block_rows), whole),
                pl.BlockSpec((jac_in.shape[0] // steps, block_rows, block_rows), lambda n, *refs: (n, 0, 0)),
                pl.BlockSpec((jac_out.shape[0] // steps, block_rows, block_rows), lambda n, *refs: (n, 0, 0)),
            ],
            out_specs=pl.BlockSpec((num_blocks, objectives, block_rows), whole),
        ),
        out_shape=jax.ShapeDtypeStruct((num_blocks, objectives, block_rows), jnp.float32),
        interpret=interpret,
    )(*tables, blocks, faces, jac_in, jac_out)


def face_exchange(psi_b, face_blocks):
    n_blk = lax.axis_size("blk")
    n_span = lax.axis_size("span")
    head = psi_b[:face_blocks]
    tail = psi_b[-face_blocks:]
    if n_blk == 2:
        passage = lax.ppermute(jnp.concatenate([tail, head], axis=0), "blk", ring(2, 1))
    else:
        prev_face = lax.ppermute(tail, "blk", ring(n_blk, 1))
        next_face = lax.ppermute(head, "blk", ring(n_blk, -1))
        passage = jnp.concatenate([prev_face, next_face], axis=0)
    lower = lax.ppermute(tail, "span", [(i, i + 1) for i in range(n_span - 1)])
    upper = lax.ppermute(head, "span", [(i + 1, i) for i in range(n_span - 1)])
    return jnp.concatenate([passage, lower, upper], axis=0)


def ordered_sum(value, axis):
    count = lax.axis_size(axis)
    me = lax.axis_index(axis)
    slots = [None] * count
    pieces = [value] + [lax.ppermute(value, axis, ring(count, k)) for k in range(1, count)]
    for place in range(count):
        pick = jnp.zeros_like(value)
        for k in range(count):
            pick = jnp.where((me - k) % count == place, pieces[k], pick)
        slots[place] = pick
    while len(slots) > 1:
        slots = [slots[i] + slots[i + 1] if i + 1 < len(slots) else slots[i] for i in range(0, len(slots), 2)]
    return slots[0]


def gather_half(half, first_axis):
    n1 = lax.axis_size(first_axis)
    return [half] + [lax.ppermute(half, first_axis, ring(n1, k)) for k in range(1, n1)]


def spread_half(gathered, second_axis, weight_of):
    n1 = len(gathered)
    n2 = lax.axis_size(second_axis)
    wide = [g.astype(jnp.float32) for g in gathered]
    own = None
    received = []
    for k2 in range(n2):
        part = None
        for k in range(n1):
            term = weight_of(k, k2) * wide[k]
            part = term if part is None else part + term
        if k2 == 0:
            own = part
        else:
            received.append(lax.ppermute(part.astype(jnp.bfloat16), second_axis, ring(n2, k2)))
    total = own
    for r in received:
        total = total + r.astype(jnp.float32)
    return total


def on_device(
    source,
    jac_interior,
    interior_rows,
    interior_cols,
    jac_face,
    face_rows,
    face_cols,
    face_map,
    frequency,
    surf_mode,
    surf_row,
    surf_node,
    mode_shape,
):
    objectives = source.shape[1]
    columns = source.shape[2]
    block_rows = jac_interior.shape[2]
    num_blocks = columns // block_rows
    face_blocks = face_map.shape[0] // 2
    nz = lax.axis_size("iz")
    ny = lax.axis_size("iy")
    inst_count = nz * ny
    iz = lax.axis_index("iz")
    iy = lax.axis_index("iy")
    face_count = jac_face.shape[1]
    passage_count = face_map.shape[0]
    outer_cols = jnp.clip(face_cols[0], 0, face_count - 1)
    mapped = jnp.clip(face_map[jnp.clip(outer_cols, 0, passage_count - 1)], 0, passage_count - 1)
    tables = (
        jnp.clip(interior_rows[0], 0, num_blocks - 1),
        jnp.clip(interior_cols[0], 0, num_blocks - 1),
        jnp.clip(face_rows[0], 0, num_blocks - 1),
        jnp.where(outer_cols < passage_count, mapped, outer_cols),
    )
    step_rate = frequency[0]
    mode_full = lax.all_gather(mode_shape, "blk", axis=0, tiled=True)

    def to_blocks(a):
        return a.reshape(objectives, num_blocks, block_rows).transpose(1, 0, 2)

    source_b = to_blocks(source[0])
    source_wide = source_b.astype(jnp.float32)

    def w_a(k, k2):
        j = ((iz - k) % nz) * ny + iy
        i = iz * ny + (iy + k2) % ny
        return loop_weight((j - i).astype(jnp.float32), inst_count)

    def w_b(k, k2):
        j = iz * ny + (iy - k) % ny
        i = ((iz + k2) % nz) * ny + iy
        return loop_weight((j - i).astype(jnp.float32), inst_count)

    half_at = num_blocks // 2
    psi_b = source_b
    for sweep_step in range(ITERS):
        face_raw = face_exchange(psi_b, face_blocks)
        got_a = gather_half(psi_b[:half_at], "iz")
        got_b = gather_half(psi_b[half_at:], "iy")
        local = local_sweep(tables, psi_b, face_raw, jac_interior[0], jac_face[0])
        got_a, got_b, local = lax.optimization_barrier((got_a, got_b, local))
        spec_a = spread_half(got_a, "iy", w_a)
        spec_b = spread_half(got_b, "iz", w_b)
        spectral = jnp.concatenate([spec_a, spec_b], axis=0)
        psi_b = (source_wide - local - step_rate * spectral).astype(jnp.bfloat16)
    psi_now = psi_b.transpose(1, 0, 2).reshape(objectives, columns)
    loads = psi_now[:, surf_row[0]].astype(jnp.float32)
    entry_modes = surf_mode[:, 0]
    entry_nodes = surf_node[0]
    total_modes = mode_full.shape[0]
    shape_vals = mode_full[entry_modes, entry_nodes]
    mode_table = (entry_modes[:, None] == jnp.arange(total_modes)[None, :]).astype(jnp.float32)
    owner_table = mode_table * shape_vals[:, None]
    contrib = jnp.einsum("re,em->mr", loads, owner_table, precision=lax.Precision.HIGHEST)
    contrib = ordered_sum(ordered_sum(contrib, "blk"), "span")
    mode_dev = mode_shape.shape[0]
    own_modes = lax.dynamic_slice_in_dim(contrib, lax.axis_index("blk") * mode_dev, mode_dev, axis=0)
    return (psi_now[None], own_modes[None])


def solution(mesh):
    n_blk, n_span, n_inst = (mesh.shape[a] for a in ("blk", "span", "inst"))
    rows = INST_ROWS if n_inst % INST_ROWS == 0 else 1
    devices = np.asarray(mesh.devices).reshape(n_blk, n_span, rows, n_inst // rows)
    grid = Mesh(devices, ("blk", "span", "iz", "iy"))
    inst = ("iz", "iy")
    dev = ("blk", "span", "iz", "iy")
    return jax.shard_map(
        on_device,
        mesh=grid,
        in_specs=(
            P(inst, None, ("blk", "span")),
            P(dev, None, None, None),
            P(dev, None),
            P(dev, None),
            P(dev, None, None, None),
            P(dev, None),
            P(dev, None),
            P(),
            P(),
            P(dev, None),
            P(dev, None),
            P(dev, None),
            P("blk", None),
        ),
        out_specs=(P(inst, None, ("blk", "span")), P(inst, "blk", None)),
        check_vma=False,
    )
```

```python
import math

import jax
import jax.numpy as jnp
import numpy as np
from jax import lax
from jax.experimental import pallas as pl
from jax.experimental.pallas import tpu as pltpu
from jax.sharding import Mesh
from jax.sharding import PartitionSpec as P

ITERS = 6
INST_ROWS = 4


def ring(count, shift):
    return [(i, (i + shift) % count) for i in range(count)]


def loop_weight(offset, inst_count):
    angle = math.pi * offset / inst_count
    parity = jnp.cos(math.pi * offset)
    sine_safe = jnp.where(offset == 0, 1.0, jnp.sin(angle))
    value = 0.5 * parity / sine_safe
    return jnp.where(offset == 0, 0.0, value)


def block_sweep(blocks, block_cols, jacobians, row_table):
    picked = blocks[block_cols]
    products = jnp.einsum("nrk,nkl->nrl", picked, jacobians, preferred_element_type=jnp.float32)
    return jnp.einsum("nrl,nb->brl", products, row_table, precision=lax.Precision.HIGHEST)


def local_kernel(rows_in, cols_in, rows_out, cols_out, psi_ref, passage_ref, lower_ref, upper_ref, jin_ref, jout_ref, out_ref):
    n = pl.program_id(0)
    n_pass, n_low, n_up = passage_ref.shape[0], lower_ref.shape[0], upper_ref.shape[0]

    @pl.when(n == 0)
    def _():
        out_ref[...] = jnp.zeros_like(out_ref)

    def own_block(col):
        return psi_ref[col]

    def face_block(col):
        passage = passage_ref[jnp.clip(col, 0, n_pass - 1)]
        lower = lower_ref[jnp.clip(col - n_pass, 0, n_low - 1)]
        upper = upper_ref[jnp.clip(col - n_pass - n_low, 0, n_up - 1)]
        return jnp.where(col < n_pass, passage, jnp.where(col < n_pass + n_low, lower, upper))

    for rows, cols, pick, jac in ((rows_in, cols_in, own_block, jin_ref), (rows_out, cols_out, face_block, jout_ref)):
        group = jac.shape[0]
        steps = rows.shape[0] // group

        @pl.when(n < steps)
        def _():
            for g in range(group):
                at = n * group + g
                product = jnp.dot(pick(cols[at]), jac[g], preferred_element_type=jnp.float32)
                row = rows[at]
                out_ref[row] = out_ref[row] + product


def local_sweep(tables, blocks, faces, jac_in, jac_out, interpret=False):
    group_in = 2 if jac_in.shape[0] % 2 == 0 else 1
    group_out = 2 if jac_out.shape[0] % 2 == 0 else 1
    steps_in, steps_out = jac_in.shape[0] // group_in, jac_out.shape[0] // group_out
    block_rows = jac_in.shape[1]
    num_blocks, objectives = blocks.shape[0], blocks.shape[1]
    whole = lambda n, *refs: (0, 0, 0)
    face_specs = [pl.BlockSpec(f.shape, whole) for f in faces]
    return pl.pallas_call(
        local_kernel,
        grid_spec=pltpu.PrefetchScalarGridSpec(
            num_scalar_prefetch=4,
            grid=(max(steps_in, steps_out),),
            in_specs=[pl.BlockSpec((num_blocks, objectives, block_rows), whole)]
            + face_specs
            + [
                pl.BlockSpec((group_in, block_rows, block_rows), lambda n, *refs: (jnp.minimum(n, steps_in - 1), 0, 0)),
                pl.BlockSpec((group_out, block_rows, block_rows), lambda n, *refs: (jnp.minimum(n, steps_out - 1), 0, 0)),
            ],
            out_specs=pl.BlockSpec((num_blocks, objectives, block_rows), whole),
        ),
        out_shape=jax.ShapeDtypeStruct((num_blocks, objectives, block_rows), jnp.float32),
        interpret=interpret,
    )(*tables, blocks, *faces, jac_in, jac_out)


def face_exchange(psi_b, face_blocks):
    n_blk = lax.axis_size("blk")
    n_span = lax.axis_size("span")
    head = psi_b[:face_blocks]
    tail = psi_b[-face_blocks:]
    if n_blk == 2:
        passage = lax.ppermute(jnp.concatenate([tail, head], axis=0), "blk", ring(2, 1))
    else:
        prev_face = lax.ppermute(tail, "blk", ring(n_blk, 1))
        next_face = lax.ppermute(head, "blk", ring(n_blk, -1))
        passage = jnp.concatenate([prev_face, next_face], axis=0)
    lower = lax.ppermute(tail, "span", [(i, i + 1) for i in range(n_span - 1)])
    upper = lax.ppermute(head, "span", [(i + 1, i) for i in range(n_span - 1)])
    return passage, lower, upper


def ordered_sum(value, axis):
    count = lax.axis_size(axis)
    me = lax.axis_index(axis)
    slots = [None] * count
    pieces = [value] + [lax.ppermute(value, axis, ring(count, k)) for k in range(1, count)]
    for place in range(count):
        pick = jnp.zeros_like(value)
        for k in range(count):
            pick = jnp.where((me - k) % count == place, pieces[k], pick)
        slots[place] = pick
    while len(slots) > 1:
        slots = [slots[i] + slots[i + 1] if i + 1 < len(slots) else slots[i] for i in range(0, len(slots), 2)]
    return slots[0]


def gather_half(half, first_axis):
    n1 = lax.axis_size(first_axis)
    return [half] + [lax.ppermute(half, first_axis, ring(n1, k)) for k in range(1, n1)]


def spread_half(gathered, second_axis, weight_of):
    n1 = len(gathered)
    n2 = lax.axis_size(second_axis)
    wide = [g.astype(jnp.float32) for g in gathered]
    own = None
    received = []
    for k2 in range(n2):
        part = None
        for k in range(n1):
            term = weight_of(k, k2) * wide[k]
            part = term if part is None else part + term
        if k2 == 0:
            own = part
        else:
            received.append(lax.ppermute(part.astype(jnp.bfloat16), second_axis, ring(n2, k2)))
    total = own
    for r in received:
        total = total + r.astype(jnp.float32)
    return total


def on_device(
    source,
    jac_interior,
    interior_rows,
    interior_cols,
    jac_face,
    face_rows,
    face_cols,
    face_map,
    frequency,
    surf_mode,
    surf_row,
    surf_node,
    mode_shape,
):
    objectives = source.shape[1]
    columns = source.shape[2]
    block_rows = jac_interior.shape[2]
    num_blocks = columns // block_rows
    face_blocks = face_map.shape[0] // 2
    nz = lax.axis_size("iz")
    ny = lax.axis_size("iy")
    inst_count = nz * ny
    iz = lax.axis_index("iz")
    iy = lax.axis_index("iy")
    face_count = jac_face.shape[1]
    passage_count = face_map.shape[0]
    outer_cols = jnp.clip(face_cols[0], 0, face_count - 1)
    mapped = jnp.clip(face_map[jnp.clip(outer_cols, 0, passage_count - 1)], 0, passage_count - 1)
    tables = (
        jnp.clip(interior_rows[0], 0, num_blocks - 1),
        jnp.clip(interior_cols[0], 0, num_blocks - 1),
        jnp.clip(face_rows[0], 0, num_blocks - 1),
        jnp.where(outer_cols < passage_count, mapped, outer_cols),
    )
    step_rate = frequency[0]
    mode_full = lax.all_gather(mode_shape, "blk", axis=0, tiled=True)

    def to_blocks(a):
        return a.reshape(objectives, num_blocks, block_rows).transpose(1, 0, 2)

    source_b = to_blocks(source[0])
    source_wide = source_b.astype(jnp.float32)

    def w_a(k, k2):
        j = ((iz - k) % nz) * ny + iy
        i = iz * ny + (iy + k2) % ny
        return loop_weight((j - i).astype(jnp.float32), inst_count)

    def w_b(k, k2):
        j = iz * ny + (iy - k) % ny
        i = ((iz + k2) % nz) * ny + iy
        return loop_weight((j - i).astype(jnp.float32), inst_count)

    half_at = num_blocks // 2
    psi_b = source_b
    for sweep_step in range(ITERS):
        face_raw = face_exchange(psi_b, face_blocks)
        got_a = gather_half(psi_b[:half_at], "iz")
        got_b = gather_half(psi_b[half_at:], "iy")
        local = local_sweep(tables, psi_b, face_raw, jac_interior[0], jac_face[0])
        got_a, got_b, local = lax.optimization_barrier((got_a, got_b, local))
        spec_a = spread_half(got_a, "iy", w_a)
        spec_b = spread_half(got_b, "iz", w_b)
        spectral = jnp.concatenate([spec_a, spec_b], axis=0)
        psi_b = (source_wide - local - step_rate * spectral).astype(jnp.bfloat16)
    psi_now = psi_b.transpose(1, 0, 2).reshape(objectives, columns)
    loads = psi_now[:, surf_row[0]].astype(jnp.float32)
    entry_modes = surf_mode[:, 0]
    entry_nodes = surf_node[0]
    total_modes = mode_full.shape[0]
    shape_vals = mode_full[entry_modes, entry_nodes]
    mode_table = (entry_modes[:, None] == jnp.arange(total_modes)[None, :]).astype(jnp.float32)
    owner_table = mode_table * shape_vals[:, None]
    contrib = jnp.einsum("re,em->mr", loads, owner_table, precision=lax.Precision.HIGHEST)
    contrib = ordered_sum(ordered_sum(contrib, "blk"), "span")
    mode_dev = mode_shape.shape[0]
    own_modes = lax.dynamic_slice_in_dim(contrib, lax.axis_index("blk") * mode_dev, mode_dev, axis=0)
    return (psi_now[None], own_modes[None])


def solution(mesh):
    n_blk, n_span, n_inst = (mesh.shape[a] for a in ("blk", "span", "inst"))
    rows = INST_ROWS if n_inst % INST_ROWS == 0 else 1
    devices = np.asarray(mesh.devices).reshape(n_blk, n_span, rows, n_inst // rows)
    grid = Mesh(devices, ("blk", "span", "iz", "iy"))
    inst = ("iz", "iy")
    dev = ("blk", "span", "iz", "iy")
    return jax.shard_map(
        on_device,
        mesh=grid,
        in_specs=(
            P(inst, None, ("blk", "span")),
            P(dev, None, None, None),
            P(dev, None),
            P(dev, None),
            P(dev, None, None, None),
            P(dev, None),
            P(dev, None),
            P(),
            P(),
            P(dev, None),
            P(dev, None),
            P(dev, None),
            P("blk", None),
        ),
        out_specs=(P(inst, None, ("blk", "span")), P(inst, "blk", None)),
        check_vma=False,
    )
```

```python
import math

import jax
import jax.numpy as jnp
import numpy as np
from jax import lax
from jax.experimental import pallas as pl
from jax.experimental.pallas import tpu as pltpu
from jax.sharding import Mesh
from jax.sharding import PartitionSpec as P

ITERS = 6
INST_ROWS = 4


def ring(count, shift):
    return [(i, (i + shift) % count) for i in range(count)]


def loop_weight(offset, inst_count):
    angle = math.pi * offset / inst_count
    parity = jnp.cos(math.pi * offset)
    sine_safe = jnp.where(offset == 0, 1.0, jnp.sin(angle))
    value = 0.5 * parity / sine_safe
    return jnp.where(offset == 0, 0.0, value)


def block_sweep(blocks, block_cols, jacobians, row_table):
    picked = blocks[block_cols]
    products = jnp.einsum("nrk,nkl->nrl", picked, jacobians, preferred_element_type=jnp.float32)
    return jnp.einsum("nrl,nb->brl", products, row_table, precision=lax.Precision.HIGHEST)


def local_kernel(rows_in, cols_in, rows_out, cols_out, psi_ref, passage_ref, lower_ref, upper_ref, jin_ref, jout_ref, out_ref):
    n = pl.program_id(0)
    n_pass, n_low, n_up = passage_ref.shape[0], lower_ref.shape[0], upper_ref.shape[0]

    @pl.when(n == 0)
    def _():
        out_ref[...] = jnp.zeros_like(out_ref)

    def own_block(col):
        return psi_ref[col]

    def face_block(col):
        passage = passage_ref[jnp.clip(col, 0, n_pass - 1)]
        lower = lower_ref[jnp.clip(col - n_pass, 0, n_low - 1)]
        upper = upper_ref[jnp.clip(col - n_pass - n_low, 0, n_up - 1)]
        return jnp.where(col < n_pass, passage, jnp.where(col < n_pass + n_low, lower, upper))

    for rows, cols, pick, jac in ((rows_in, cols_in, own_block, jin_ref), (rows_out, cols_out, face_block, jout_ref)):
        group = jac.shape[0]
        steps = rows.shape[0] // group

        @pl.when(n < steps)
        def _():
            for g in range(group):
                at = n * group + g
                product = jnp.dot(pick(cols[at]), jac[g], preferred_element_type=jnp.float32)
                row = rows[at]
                out_ref[row] = out_ref[row] + product


def local_sweep(tables, blocks, faces, jac_in, jac_out, interpret=False):
    steps = math.gcd(jac_in.shape[0], jac_out.shape[0])
    group_in, group_out = jac_in.shape[0] // steps, jac_out.shape[0] // steps
    steps_in, steps_out = jac_in.shape[0] // group_in, jac_out.shape[0] // group_out
    block_rows = jac_in.shape[1]
    num_blocks, objectives = blocks.shape[0], blocks.shape[1]
    whole = lambda n, *refs: (0, 0, 0)
    face_specs = [pl.BlockSpec(f.shape, whole) for f in faces]
    return pl.pallas_call(
        local_kernel,
        grid_spec=pltpu.PrefetchScalarGridSpec(
            num_scalar_prefetch=4,
            grid=(max(steps_in, steps_out),),
            in_specs=[pl.BlockSpec((num_blocks, objectives, block_rows), whole)]
            + face_specs
            + [
                pl.BlockSpec((group_in, block_rows, block_rows), lambda n, *refs: (jnp.minimum(n, steps_in - 1), 0, 0)),
                pl.BlockSpec((group_out, block_rows, block_rows), lambda n, *refs: (jnp.minimum(n, steps_out - 1), 0, 0)),
            ],
            out_specs=pl.BlockSpec((num_blocks, objectives, block_rows), whole),
        ),
        out_shape=jax.ShapeDtypeStruct((num_blocks, objectives, block_rows), jnp.float32),
        interpret=interpret,
    )(*tables, blocks, *faces, jac_in, jac_out)


def face_exchange(psi_b, face_blocks):
    n_blk = lax.axis_size("blk")
    n_span = lax.axis_size("span")
    head = psi_b[:face_blocks]
    tail = psi_b[-face_blocks:]
    if n_blk == 2:
        passage = lax.ppermute(jnp.concatenate([tail, head], axis=0), "blk", ring(2, 1))
    else:
        prev_face = lax.ppermute(tail, "blk", ring(n_blk, 1))
        next_face = lax.ppermute(head, "blk", ring(n_blk, -1))
        passage = jnp.concatenate([prev_face, next_face], axis=0)
    lower = lax.ppermute(tail, "span", [(i, i + 1) for i in range(n_span - 1)])
    upper = lax.ppermute(head, "span", [(i + 1, i) for i in range(n_span - 1)])
    return passage, lower, upper


def ordered_sum(value, axis):
    count = lax.axis_size(axis)
    me = lax.axis_index(axis)
    slots = [None] * count
    pieces = [value] + [lax.ppermute(value, axis, ring(count, k)) for k in range(1, count)]
    for place in range(count):
        pick = jnp.zeros_like(value)
        for k in range(count):
            pick = jnp.where((me - k) % count == place, pieces[k], pick)
        slots[place] = pick
    while len(slots) > 1:
        slots = [slots[i] + slots[i + 1] if i + 1 < len(slots) else slots[i] for i in range(0, len(slots), 2)]
    return slots[0]


def gather_half(half, first_axis):
    n1 = lax.axis_size(first_axis)
    return [half] + [lax.ppermute(half, first_axis, ring(n1, k)) for k in range(1, n1)]


def spread_half(gathered, second_axis, weight_of):
    n1 = len(gathered)
    n2 = lax.axis_size(second_axis)
    wide = [g.astype(jnp.float32) for g in gathered]
    own = None
    received = []
    for k2 in range(n2):
        part = None
        for k in range(n1):
            term = weight_of(k, k2) * wide[k]
            part = term if part is None else part + term
        if k2 == 0:
            own = part
        else:
            received.append(lax.ppermute(part.astype(jnp.bfloat16), second_axis, ring(n2, k2)))
    total = own
    for r in received:
        total = total + r.astype(jnp.float32)
    return total


def on_device(
    source,
    jac_interior,
    interior_rows,
    interior_cols,
    jac_face,
    face_rows,
    face_cols,
    face_map,
    frequency,
    surf_mode,
    surf_row,
    surf_node,
    mode_shape,
):
    objectives = source.shape[1]
    columns = source.shape[2]
    block_rows = jac_interior.shape[2]
    num_blocks = columns // block_rows
    face_blocks = face_map.shape[0] // 2
    nz = lax.axis_size("iz")
    ny = lax.axis_size("iy")
    inst_count = nz * ny
    iz = lax.axis_index("iz")
    iy = lax.axis_index("iy")
    face_count = jac_face.shape[1]
    passage_count = face_map.shape[0]
    outer_cols = jnp.clip(face_cols[0], 0, face_count - 1)
    mapped = jnp.clip(face_map[jnp.clip(outer_cols, 0, passage_count - 1)], 0, passage_count - 1)
    tables = (
        jnp.clip(interior_rows[0], 0, num_blocks - 1),
        jnp.clip(interior_cols[0], 0, num_blocks - 1),
        jnp.clip(face_rows[0], 0, num_blocks - 1),
        jnp.where(outer_cols < passage_count, mapped, outer_cols),
    )
    step_rate = frequency[0]
    mode_full = lax.all_gather(mode_shape, "blk", axis=0, tiled=True)

    def to_blocks(a):
        return a.reshape(objectives, num_blocks, block_rows).transpose(1, 0, 2)

    source_b = to_blocks(source[0])
    source_wide = source_b.astype(jnp.float32)

    def w_a(k, k2):
        j = ((iz - k) % nz) * ny + iy
        i = iz * ny + (iy + k2) % ny
        return loop_weight((j - i).astype(jnp.float32), inst_count)

    def w_b(k, k2):
        j = iz * ny + (iy - k) % ny
        i = ((iz + k2) % nz) * ny + iy
        return loop_weight((j - i).astype(jnp.float32), inst_count)

    half_at = num_blocks // 2
    psi_b = source_b
    for sweep_step in range(ITERS):
        face_raw = face_exchange(psi_b, face_blocks)
        got_a = gather_half(psi_b[:half_at], "iz")
        got_b = gather_half(psi_b[half_at:], "iy")
        local = local_sweep(tables, psi_b, face_raw, jac_interior[0], jac_face[0])
        got_a, got_b, local = lax.optimization_barrier((got_a, got_b, local))
        spec_a = spread_half(got_a, "iy", w_a)
        spec_b = spread_half(got_b, "iz", w_b)
        spectral = jnp.concatenate([spec_a, spec_b], axis=0)
        psi_b = (source_wide - local - step_rate * spectral).astype(jnp.bfloat16)
    psi_now = psi_b.transpose(1, 0, 2).reshape(objectives, columns)
    loads = psi_now[:, surf_row[0]].astype(jnp.float32)
    entry_modes = surf_mode[:, 0]
    entry_nodes = surf_node[0]
    total_modes = mode_full.shape[0]
    shape_vals = mode_full[entry_modes, entry_nodes]
    mode_table = (entry_modes[:, None] == jnp.arange(total_modes)[None, :]).astype(jnp.float32)
    owner_table = mode_table * shape_vals[:, None]
    contrib = jnp.einsum("re,em->mr", loads, owner_table, precision=lax.Precision.HIGHEST)
    contrib = ordered_sum(ordered_sum(contrib, "blk"), "span")
    mode_dev = mode_shape.shape[0]
    own_modes = lax.dynamic_slice_in_dim(contrib, lax.axis_index("blk") * mode_dev, mode_dev, axis=0)
    return (psi_now[None], own_modes[None])


def solution(mesh):
    n_blk, n_span, n_inst = (mesh.shape[a] for a in ("blk", "span", "inst"))
    rows = INST_ROWS if n_inst % INST_ROWS == 0 else 1
    devices = np.asarray(mesh.devices).reshape(n_blk, n_span, rows, n_inst // rows)
    grid = Mesh(devices, ("blk", "span", "iz", "iy"))
    inst = ("iz", "iy")
    dev = ("blk", "span", "iz", "iy")
    return jax.shard_map(
        on_device,
        mesh=grid,
        in_specs=(
            P(inst, None, ("blk", "span")),
            P(dev, None, None, None),
            P(dev, None),
            P(dev, None),
            P(dev, None, None, None),
            P(dev, None),
            P(dev, None),
            P(),
            P(),
            P(dev, None),
            P(dev, None),
            P(dev, None),
            P("blk", None),
        ),
        out_specs=(P(inst, None, ("blk", "span")), P(inst, "blk", None)),
        check_vma=False,
    )
```
